256 devices in a mesh: gx: 16 (over x, z_hi, core), gy: 4 (over z_lo), gz: 4 (over y).
Axes of the slice: x: 4, y: 4, z: 8 (z_hi: 2, z_lo: 4; z = z_hi * 4 + z_lo), core: 2. Of those that a mesh axis runs over, the one named last changes fastest.
Arguments:
- image_slab: float32 [64, 1024, 1024], P(('gz', 'gx'), None, 'gy'), may hold values from -6 to 6
- deformed_slab: float32 [64, 1024, 1024], P(('gz', 'gx'), None, 'gy'), may hold values from -6 to 6
- shifts: int32 [2, 3, 4, 16, 4], P(None, None, 'gz', 'gx', 'gy'), may hold values from -8 to 8, as said below
Outputs:
- displacement: float32 [3, 12, 144, 132], P(None, 'gz', 'gx', 'gy')
- residual_map: float32 [64, 1024, 1024], P('gz', 'gx', 'gy')
The draws below stay inside these ranges and needn't reach their ends.
Inputs may be any that keep to these rules, and one draw needn't show every extreme that they name: `shifts`: every component lies within -8 to 8, and both ends are taken by some entry.
All inputs are finite; a program needn't handle non-finite values.
Results may differ from the reference program's by a relative error of at most 0.0003.
Values sent between devices are 32-bit elements; how exact they have to be, the bound alone decides.
No kernel may reach another device: no remote copies, remote signals or barrier semaphores. Data moves between devices by JAX's collectives and lax.ppermute only.
A program may use at most 128 MiB of HBM per device.

```python
import jax
import jax.numpy as jnp
from jax import lax

BAND = 64
BX = 64
BY = 256
ELEMENT = 8
DMAX = 8
ITERS = 2
SWEEPS = 3
BZ = 16
NX = 1024
NY = 1024
EZ = 2
EX = 8
EY = 32
N_GX = 16
N_GY = 4
N_GZ = 4


def draw_shifts(key, part):
    total_count = ITERS * 3 * N_GZ * N_GX * N_GY
    key_values, key_high, key_low = jax.random.split(key, 3)
    values = jax.random.randint(key_values, (total_count,), -DMAX, DMAX + 1, dtype=jnp.int32)
    high_spot = jax.random.randint(key_high, (), 0, total_count, dtype=jnp.int32)
    low_spot = (high_spot + jax.random.randint(key_low, (), 1, total_count, dtype=jnp.int32)) % total_count
    values = values.at[high_spot].set(DMAX).at[low_spot].set(-DMAX)
    return values.reshape(ITERS, 3, N_GZ, N_GX, N_GY)


def steps_of(key, extent, pieces, least, top_value):
    def one(axis_at, blocks):
        heights = jax.random.uniform(jax.random.fold_in(jax.random.fold_in(key, 6), axis_at), (blocks,), jnp.float32, least / len(pieces), top_value / len(pieces))
        return jnp.repeat(jnp.exp(heights), extent[axis_at] // blocks).reshape((-1,) + (1,) * (len(extent) - axis_at - 1))

    gain = one(*pieces[0])
    for cut in pieces[1:]:
        gain = gain * one(*cut)
    return gain


def noise(rng, dims, spread, limit, pieces=(), kind=jnp.bfloat16):
    entries = spread * jax.random.normal(rng, dims, jnp.float32)
    if pieces:
        entries = entries * steps_of(rng, dims, pieces, -0.22, 0.18)
    return jnp.clip(entries, -limit, limit).astype(kind)


def setup_inputs(seed: int = 0) -> dict:
    key_of = jax.random.split(jax.random.key(seed), 4)
    return {
        "image_slab": noise(key_of[0], (BAND, NX, NY), 1.0, 6.0, ((0, 64), (2, 4)), jnp.float32),
        "deformed_slab": noise(key_of[1], (BAND, NX, NY), 1.0, 6.0, ((0, 64), (2, 4)), jnp.float32),
        "shifts": draw_shifts(jax.random.fold_in(key_of[3], 71), 0),
    }


DAMPING = 0.7
REGULARIZE = 4.0


def shape_table(voxel_count, elem_size):
    voxel_index = jnp.arange(voxel_count, dtype=jnp.int32)
    fraction = ((voxel_index % elem_size).astype(jnp.float32) + 0.5) / elem_size
    owning = voxel_index // elem_size
    node_index = jnp.arange(voxel_count // elem_size + 1, dtype=jnp.int32)
    lower_part = (node_index[None, :] == owning[:, None]).astype(jnp.float32) * (1.0 - fraction)[:, None]
    upper_part = (node_index[None, :] == owning[:, None] + 1).astype(jnp.float32) * fraction[:, None]
    return lower_part + upper_part


def cut_range(array, axis, start, length):
    return lax.slice_in_dim(array, start, start + length, axis=axis)


def smooth(array, axis):
    length = array.shape[axis] - 2
    return (cut_range(array, axis, 0, length) + 2.0 * cut_range(array, axis, 1, length) + cut_range(array, axis, 2, length)) * 0.25


def differ(array, axis):
    length = array.shape[axis] - 2
    return (cut_range(array, axis, 2, length) - cut_range(array, axis, 0, length)) * 0.5


def gradients(extended):
    along_z = smooth(smooth(differ(extended, 0), 1), 2)
    along_x = smooth(smooth(differ(extended, 1), 0), 2)
    along_y = smooth(smooth(differ(extended, 2), 0), 1)
    return jnp.stack([along_z, along_x, along_y])


def interpolate(nodal, table_z, table_x, table_y):
    hi = lax.Precision.HIGHEST
    step = jnp.einsum("cpaqbrd,yd->cpaqbry", nodal, table_y, precision=hi)
    step = jnp.einsum("cpaqbry,xb->cpaqxry", step, table_x, precision=hi)
    return jnp.einsum("cpaqxry,za->cpzqxry", step, table_z, precision=hi)


def restrict(field, table_z, table_x, table_y):
    hi = lax.Precision.HIGHEST
    step = jnp.einsum("cpzqxry,za->cpaqxry", field, table_z, precision=hi)
    step = jnp.einsum("cpaqxry,xb->cpaqbry", step, table_x, precision=hi)
    return jnp.einsum("cpaqbry,yd->cpaqbrd", step, table_y, precision=hi)


def share_axis(partial_value, axis, groups, elems):
    moved = jnp.moveaxis(partial_value, (axis, axis + 1), (0, 1))
    remain = moved.shape[2:]
    main_part = moved[:, :elems].reshape((groups * elems,) + remain)
    unique = jnp.concatenate([main_part, jnp.zeros((1,) + remain, moved.dtype)], 0)
    targets = (elems * jnp.arange(1, groups + 1, dtype=jnp.int32)).astype(jnp.int32)
    unique = unique.at[targets].add(moved[:, elems])
    gather_index = (elems * jnp.arange(groups, dtype=jnp.int32)[:, None] + jnp.arange(elems + 1, dtype=jnp.int32)[None, :]).astype(jnp.int32)
    back = unique[gather_index]
    return jnp.moveaxis(back, (0, 1), (axis, axis + 1))


def share(partial_value):
    total = share_axis(partial_value, 1, N_GZ, EZ)
    total = share_axis(total, 3, N_GX, EX)
    return share_axis(total, 5, N_GY, EY)


def invert(diag):
    a, b, c, d, e, f = diag[0], diag[1], diag[2], diag[3], diag[4], diag[5]
    i00 = b * c - f * f
    i11 = a * c - e * e
    i22 = a * b - d * d
    i01 = e * f - d * c
    i02 = d * f - b * e
    i12 = d * e - a * f
    det = a * i00 + d * i01 + e * i02
    return jnp.stack([i00, i11, i22, i01, i02, i12]) / det


def apply_inverse(inverse, vector):
    out_z = inverse[0] * vector[0] + inverse[3] * vector[1] + inverse[4] * vector[2]
    out_x = inverse[3] * vector[0] + inverse[1] * vector[1] + inverse[5] * vector[2]
    out_y = inverse[4] * vector[0] + inverse[5] * vector[1] + inverse[2] * vector[2]
    return jnp.stack([out_z, out_x, out_y])


def bricked(field):
    return field.reshape(field.shape[0], N_GZ, BZ, N_GX, BX, N_GY, BY)


def reference(image_slab, deformed_slab, shifts):
    table_z = shape_table(BZ, ELEMENT)
    table_x = shape_table(BX, ELEMENT)
    table_y = shape_table(BY, ELEMENT)
    grads = bricked(gradients(jnp.pad(image_slab, 1)))
    image = bricked(image_slab[None])[0]
    padded = jnp.pad(deformed_slab, DMAX)
    brick_count = N_GZ * N_GX * N_GY
    flat_index = jnp.arange(brick_count, dtype=jnp.int32)

    def warp_all(iteration):
        def fetch(index):
            brick_z = index // (N_GX * N_GY)
            brick_x = (index // N_GY) % N_GX
            brick_y = index % N_GY
            offset = shifts[iteration, :, brick_z, brick_x, brick_y]
            starts = (brick_z * BZ + DMAX + offset[0], brick_x * BX + DMAX + offset[1], brick_y * BY + DMAX + offset[2])
            return lax.dynamic_slice(padded, [s.astype(jnp.int32) for s in starts], (BZ, BX, BY))
        blocks = lax.map(fetch, flat_index)
        return blocks.reshape(N_GZ, N_GX, N_GY, BZ, BX, BY).transpose(0, 3, 1, 4, 2, 5)

    def shift_field(iteration):
        values = shifts[iteration].astype(jnp.float32)
        return values[:, :, None, :, None, :, None]

    def residual(nodal, warped, iteration):
        moved = interpolate(nodal, table_z, table_x, table_y)
        return image - warped - jnp.sum(grads * (moved - shift_field(iteration)), axis=0)

    pairs = ((0, 0), (1, 1), (2, 2), (0, 1), (0, 2), (1, 2))
    products = jnp.stack([grads[i] * grads[j] for i, j in pairs])
    diag = share(restrict(products, table_z * table_z, table_x * table_x, table_y * table_y))
    diag = diag + REGULARIZE * jnp.array([1.0, 1.0, 1.0, 0.0, 0.0, 0.0], diag.dtype)[:, None, None, None, None, None, None]
    inverse = invert(diag)
    nodal = jnp.zeros((3, N_GZ, EZ + 1, N_GX, EX + 1, N_GY, EY + 1), jnp.float32)
    warped = None
    for iteration in range(ITERS):
        warped = warp_all(iteration)
        resid = residual(nodal, warped, iteration)
        rhs = share(restrict(grads * resid[None], table_z, table_x, table_y))
        delta = DAMPING * apply_inverse(inverse, rhs)
        for sweep in range(SWEEPS - 1):
            inner = jnp.sum(grads * interpolate(delta, table_z, table_x, table_y), axis=0)
            applied = share(restrict(grads * inner[None], table_z, table_x, table_y)) + REGULARIZE * delta
            delta = delta + DAMPING * apply_inverse(inverse, rhs - applied)
        nodal = nodal + delta
    final = residual(nodal, warped, ITERS - 1)
    displacement = nodal.reshape(3, N_GZ * (EZ + 1), N_GX * (EX + 1), N_GY * (EY + 1))
    return displacement, final.reshape(BAND, NX, NY)
```

```python
import numpy as np

import jax
import jax.numpy as jnp
from jax import lax
from jax.sharding import PartitionSpec as P

ELEMENT = 8
DMAX = 8
ITERS = 2
SWEEPS = 3


DAMPING = 0.7
REGULARIZE = 4.0
HI = lax.Precision.HIGHEST


def shape_table(voxel_count, squared=False):
    voxel = np.arange(voxel_count)
    fraction = ((voxel % ELEMENT).astype(np.float32) + 0.5) / ELEMENT
    owning = voxel // ELEMENT
    nodes = np.arange(voxel_count // ELEMENT + 1)
    lower = (nodes[None, :] == owning[:, None]) * (1.0 - fraction)[:, None]
    upper = (nodes[None, :] == owning[:, None] + 1) * fraction[:, None]
    table = (lower + upper).astype(np.float32)
    if squared:
        table = table * table
    return jnp.asarray(table)


def z_weights(squared=False):
    fraction = (np.arange(ELEMENT, dtype=np.float32) + 0.5) / ELEMENT
    lower = 1.0 - fraction
    if squared:
        return lower * lower, fraction * fraction
    return lower, fraction


def neighbours(axis):
    count = lax.axis_size(axis)
    forward = [(i, i + 1) for i in range(count - 1)]
    backward = [(i + 1, i) for i in range(count - 1)]
    return forward, backward


def halo(block, axis, dim, width):
    forward, backward = neighbours(axis)
    size = block.shape[dim]
    low = lax.ppermute(lax.slice_in_dim(block, size - width, size, axis=dim), axis, forward)
    high = lax.ppermute(lax.slice_in_dim(block, 0, width, axis=dim), axis, backward)
    return jnp.concatenate([low, block, high], axis=dim)


def share(partial_value):
    value = partial_value
    for axis, dim in (("gz", 1), ("gx", 2), ("gy", 3)):
        forward, backward = neighbours(axis)
        size = value.shape[dim]
        first = lax.slice_in_dim(value, 0, 1, axis=dim)
        last = lax.slice_in_dim(value, size - 1, size, axis=dim)
        from_low = lax.ppermute(last, axis, forward)
        from_high = lax.ppermute(first, axis, backward)
        middle = lax.slice_in_dim(value, 1, size - 1, axis=dim)
        value = jnp.concatenate([first + from_low, middle, last + from_high], axis=dim)
    return value


def cut_range(array, axis, start, length):
    return lax.slice_in_dim(array, start, start + length, axis=axis)


def smooth(array, axis):
    length = array.shape[axis] - 2
    return (
        cut_range(array, axis, 0, length)
        + 2.0 * cut_range(array, axis, 1, length)
        + cut_range(array, axis, 2, length)
    ) * 0.25


def differ(array, axis):
    length = array.shape[axis] - 2
    return (cut_range(array, axis, 2, length) - cut_range(array, axis, 0, length)) * 0.5


def gradients(extended):
    along_z = smooth(smooth(differ(extended, 0), 1), 2)
    along_x = smooth(smooth(differ(extended, 1), 0), 2)
    along_y = smooth(smooth(differ(extended, 2), 0), 1)
    return jnp.stack([along_z, along_x, along_y])


def interp_xy(nodal, table_x, table_y):
    step = jnp.einsum("cabd,yd->caby", nodal, table_y, precision=HI)
    return jnp.einsum("caby,xb->caxy", step, table_x, precision=HI)


def expand_z(values, weights):
    lower, upper = weights
    count = values.shape[1] - 1
    low = values[:, :count, None]
    high = values[:, 1:, None]
    shape = (1, 1, ELEMENT, 1, 1)
    joined = low * lower.reshape(shape) + high * upper.reshape(shape)
    return joined.reshape((values.shape[0], count * ELEMENT) + values.shape[2:])


def interpolate(nodal, tables, weights):
    return expand_z(interp_xy(nodal, *tables), weights)


def reduce_z(field, weights):
    lower, upper = weights
    count = field.shape[1] // ELEMENT
    blocks = field.reshape((field.shape[0], count, ELEMENT) + field.shape[2:])
    shape = (1, 1, ELEMENT, 1, 1)
    low = jnp.sum(blocks * lower.reshape(shape), axis=2)
    high = jnp.sum(blocks * upper.reshape(shape), axis=2)
    parts = [low[:, :1]]
    for e in range(1, count):
        parts.append(high[:, e - 1 : e] + low[:, e : e + 1])
    parts.append(high[:, count - 1 :])
    return jnp.concatenate(parts, axis=1)


def restrict(field, tables, weights):
    table_x, table_y = tables
    step = reduce_z(field, weights)
    step = jnp.einsum("caxy,xb->caby", step, table_x, precision=HI)
    return jnp.einsum("caby,yd->cabd", step, table_y, precision=HI)


def invert(diag):
    a, b, c, d, e, f = (diag[0], diag[1], diag[2], diag[3], diag[4], diag[5])
    i00 = b * c - f * f
    i11 = a * c - e * e
    i22 = a * b - d * d
    i01 = e * f - d * c
    i02 = d * f - b * e
    i12 = d * e - a * f
    det = a * i00 + d * i01 + e * i02
    return jnp.stack([i00, i11, i22, i01, i02, i12]) / det


def apply_inverse(inverse, vector):
    out_z = inverse[0] * vector[0] + inverse[3] * vector[1] + inverse[4] * vector[2]
    out_x = inverse[3] * vector[0] + inverse[1] * vector[1] + inverse[5] * vector[2]
    out_y = inverse[4] * vector[0] + inverse[5] * vector[1] + inverse[2] * vector[2]
    return jnp.stack([out_z, out_x, out_y])


def bricks_of(image_slab, deformed_slab):
    both = jnp.concatenate([image_slab, deformed_slab], axis=0)
    both = halo(both, "gy", 2, DMAX)
    n_gx = lax.axis_size("gx")
    fields, nx, ny = both.shape
    bx = nx // n_gx
    main = both.reshape(fields, n_gx, bx, ny)
    zero = jnp.zeros((fields, 1, DMAX, ny), both.dtype)
    low = jnp.concatenate([zero, main[:, :-1, bx - DMAX :]], axis=1)
    high = jnp.concatenate([main[:, 1:, :DMAX], zero], axis=1)
    windows = jnp.concatenate([low, main, high], axis=2)
    windows = jnp.moveaxis(windows, 1, 0)
    brick = lax.all_to_all(windows, "gx", split_axis=0, concat_axis=0, tiled=True)
    image = brick[:, 0]
    deformed = brick[:, 1]
    image_ext = halo(image[:, DMAX - 1 : DMAX + bx + 1, DMAX - 1 : ny - DMAX + 1], "gz", 0, 1)
    deformed_ext = halo(deformed, "gz", 0, DMAX)
    return image_ext, deformed_ext


def shards(image_slab, deformed_slab, shifts):
    image_ext, deformed_ext = bricks_of(image_slab, deformed_slab)
    image = image_ext[1:-1, 1:-1, 1:-1]
    z_count, x_count, y_count = image.shape
    grads = gradients(image_ext)
    tables = (shape_table(x_count), shape_table(y_count))
    tables_sq = (shape_table(x_count, True), shape_table(y_count, True))
    weights = z_weights(False)
    weights_sq = z_weights(True)
    pairs = ((0, 0), (1, 1), (2, 2), (0, 1), (0, 2), (1, 2))

    def residual(moved, warped_now, offset):
        offset_float = offset.astype(jnp.float32)[:, None, None, None]
        return image - warped_now - jnp.sum(grads * (moved - offset_float), axis=0)

    def warp(iteration):
        offset = shifts[iteration, :, 0, 0, 0]
        starts = [DMAX + offset[0], DMAX + offset[1], DMAX + offset[2]]
        return lax.dynamic_slice(deformed_ext, starts, (z_count, x_count, y_count)), offset

    def operator(delta):
        inner = jnp.sum(grads * interpolate(delta, tables, weights), axis=0)
        return share(restrict(grads * inner[None], tables, weights))

    warped, offset = warp(0)
    resid = image - warped + jnp.sum(grads * offset.astype(jnp.float32)[:, None, None, None], axis=0)
    products = jnp.stack([grads[i] * grads[j] for i, j in pairs])
    first = jnp.concatenate(
        [restrict(products, tables_sq, weights_sq), restrict(grads * resid[None], tables, weights)],
        axis=0,
    )
    first = share(first)
    diag = first[:6] + REGULARIZE * jnp.array([1.0, 1.0, 1.0, 0.0, 0.0, 0.0], jnp.float32)[
        :, None, None, None
    ]
    inverse = invert(diag)
    rhs = first[6:]
    nodal = jnp.zeros((3, z_count // ELEMENT + 1, x_count // ELEMENT + 1, y_count // ELEMENT + 1), jnp.float32)
    for iteration in range(ITERS):
        if iteration > 0:
            warped, offset = warp(iteration)
            resid = residual(interpolate(nodal, tables, weights), warped, offset)
            rhs = share(restrict(grads * resid[None], tables, weights))
        delta = DAMPING * apply_inverse(inverse, rhs)
        for sweep in range(SWEEPS - 1):
            applied = operator(delta) + REGULARIZE * delta
            delta = delta + DAMPING * apply_inverse(inverse, rhs - applied)
        nodal = nodal + delta
    final = residual(interpolate(nodal, tables, weights), warped, offset)
    return (nodal, final)


def solution(mesh):
    return jax.shard_map(
        shards,
        mesh=mesh,
        in_specs=(
            P(("gz", "gx"), None, "gy"),
            P(("gz", "gx"), None, "gy"),
            P(None, None, "gz", "gx", "gy"),
        ),
        out_specs=(P(None, "gz", "gx", "gy"), P("gz", "gx", "gy")),
        check_vma=False,
    )
```

```python
import numpy as np

import jax
import jax.numpy as jnp
from jax import lax
from jax.sharding import PartitionSpec as P

ELEMENT = 8
DMAX = 8
ITERS = 2
SWEEPS = 3


DAMPING = 0.7
REGULARIZE = 4.0
HI = lax.Precision.HIGHEST


def shape_table(voxel_count, squared=False):
    voxel = np.arange(voxel_count)
    fraction = ((voxel % ELEMENT).astype(np.float32) + 0.5) / ELEMENT
    owning = voxel // ELEMENT
    nodes = np.arange(voxel_count // ELEMENT + 1)
    lower = (nodes[None, :] == owning[:, None]) * (1.0 - fraction)[:, None]
    upper = (nodes[None, :] == owning[:, None] + 1) * fraction[:, None]
    table = (lower + upper).astype(np.float32)
    if squared:
        table = table * table
    return jnp.asarray(table)


def z_weights(squared=False):
    fraction = (np.arange(ELEMENT, dtype=np.float32) + 0.5) / ELEMENT
    lower = 1.0 - fraction
    if squared:
        return lower * lower, fraction * fraction
    return lower, fraction


def neighbours(axis):
    count = lax.axis_size(axis)
    forward = [(i, i + 1) for i in range(count - 1)]
    backward = [(i + 1, i) for i in range(count - 1)]
    return forward, backward


def halo(block, axis, dim, width):
    forward, backward = neighbours(axis)
    size = block.shape[dim]
    low = lax.ppermute(lax.slice_in_dim(block, size - width, size, axis=dim), axis, forward)
    high = lax.ppermute(lax.slice_in_dim(block, 0, width, axis=dim), axis, backward)
    return jnp.concatenate([low, block, high], axis=dim)


def share(partial_value):
    value = partial_value
    for axis, dim in (("gz", 1), ("gx", 2), ("gy", 3)):
        forward, backward = neighbours(axis)
        size = value.shape[dim]
        first = lax.slice_in_dim(value, 0, 1, axis=dim)
        last = lax.slice_in_dim(value, size - 1, size, axis=dim)
        from_low = lax.ppermute(last, axis, forward)
        from_high = lax.ppermute(first, axis, backward)
        middle = lax.slice_in_dim(value, 1, size - 1, axis=dim)
        value = jnp.concatenate([first + from_low, middle, last + from_high], axis=dim)
    return value


def cut_range(array, axis, start, length):
    return lax.slice_in_dim(array, start, start + length, axis=axis)


def smooth(array, axis):
    length = array.shape[axis] - 2
    return (
        cut_range(array, axis, 0, length)
        + 2.0 * cut_range(array, axis, 1, length)
        + cut_range(array, axis, 2, length)
    ) * 0.25


def differ(array, axis):
    length = array.shape[axis] - 2
    return (cut_range(array, axis, 2, length) - cut_range(array, axis, 0, length)) * 0.5


def gradients(extended):
    along_z = smooth(smooth(differ(extended, 0), 1), 2)
    along_x = smooth(smooth(differ(extended, 1), 0), 2)
    along_y = smooth(smooth(differ(extended, 2), 0), 1)
    return jnp.stack([along_z, along_x, along_y])


def interp_xy(nodal, table_x, table_y):
    step = jnp.einsum("cabd,yd->caby", nodal, table_y, precision=HI)
    return jnp.einsum("caby,xb->caxy", step, table_x, precision=HI)


def expand_z(values, weights):
    lower, upper = weights
    count = values.shape[1] - 1
    low = values[:, :count, None]
    high = values[:, 1:, None]
    shape = (1, 1, ELEMENT, 1, 1)
    joined = low * lower.reshape(shape) + high * upper.reshape(shape)
    return joined.reshape((values.shape[0], count * ELEMENT) + values.shape[2:])


def interpolate(nodal, tables, weights):
    return expand_z(interp_xy(nodal, *tables), weights)


def reduce_z(field, weights):
    lower, upper = weights
    count = field.shape[1] // ELEMENT
    blocks = field.reshape((field.shape[0], count, ELEMENT) + field.shape[2:])
    shape = (1, 1, ELEMENT, 1, 1)
    low = jnp.sum(blocks * lower.reshape(shape), axis=2)
    high = jnp.sum(blocks * upper.reshape(shape), axis=2)
    parts = [low[:, :1]]
    for e in range(1, count):
        parts.append(high[:, e - 1 : e] + low[:, e : e + 1])
    parts.append(high[:, count - 1 :])
    return jnp.concatenate(parts, axis=1)


def restrict(field, tables, weights):
    table_x, table_y = tables
    step = reduce_z(field, weights)
    step = jnp.einsum("caxy,xb->caby", step, table_x, precision=HI)
    return jnp.einsum("caby,yd->cabd", step, table_y, precision=HI)


def invert(diag):
    a, b, c, d, e, f = (diag[0], diag[1], diag[2], diag[3], diag[4], diag[5])
    i00 = b * c - f * f
    i11 = a * c - e * e
    i22 = a * b - d * d
    i01 = e * f - d * c
    i02 = d * f - b * e
    i12 = d * e - a * f
    det = a * i00 + d * i01 + e * i02
    return jnp.stack([i00, i11, i22, i01, i02, i12]) / det


def apply_inverse(inverse, vector):
    out_z = inverse[0] * vector[0] + inverse[3] * vector[1] + inverse[4] * vector[2]
    out_x = inverse[3] * vector[0] + inverse[1] * vector[1] + inverse[5] * vector[2]
    out_y = inverse[4] * vector[0] + inverse[5] * vector[1] + inverse[2] * vector[2]
    return jnp.stack([out_z, out_x, out_y])


def bricks_of(image_slab, deformed_slab):
    both = jnp.concatenate([image_slab, deformed_slab], axis=0)
    both = halo(both, "gy", 2, DMAX)
    n_gx = lax.axis_size("gx")
    fields, nx, ny = both.shape
    bx = nx // n_gx
    main = both.reshape(fields, n_gx, bx, ny)
    zero = jnp.zeros((fields, 1, DMAX, ny), both.dtype)
    low = jnp.concatenate([zero, main[:, :-1, bx - DMAX :]], axis=1)
    high = jnp.concatenate([main[:, 1:, :DMAX], zero], axis=1)
    windows = jnp.concatenate([low, main, high], axis=2)
    windows = jnp.moveaxis(windows, 1, 0)
    brick = lax.all_to_all(windows, "gx", split_axis=0, concat_axis=0, tiled=True)
    forward, backward = neighbours("gz")
    bz = brick.shape[0]
    image = brick[:, 0]
    deformed = brick[:, 1]
    to_high = jnp.concatenate([deformed[bz - DMAX :], image[bz - 1 :]], axis=0)
    to_low = jnp.concatenate([deformed[:DMAX], image[:1]], axis=0)
    from_low = lax.ppermute(to_high, "gz", forward)
    from_high = lax.ppermute(to_low, "gz", backward)
    deformed_ext = jnp.concatenate([from_low[:DMAX], deformed, from_high[:DMAX]], axis=0)
    image_ext = jnp.concatenate([from_low[DMAX:], image, from_high[DMAX:]], axis=0)
    image_ext = image_ext[:, DMAX - 1 : DMAX + bx + 1, DMAX - 1 : ny - DMAX + 1]
    return image_ext, deformed_ext


def shards(image_slab, deformed_slab, shifts):
    image_ext, deformed_ext = bricks_of(image_slab, deformed_slab)
    image = image_ext[1:-1, 1:-1, 1:-1]
    z_count, x_count, y_count = image.shape
    grads = gradients(image_ext)
    tables = (shape_table(x_count), shape_table(y_count))
    tables_sq = (shape_table(x_count, True), shape_table(y_count, True))
    weights = z_weights(False)
    weights_sq = z_weights(True)
    pairs = ((0, 0), (1, 1), (2, 2), (0, 1), (0, 2), (1, 2))

    def residual(moved, warped_now, offset):
        offset_float = offset.astype(jnp.float32)[:, None, None, None]
        return image - warped_now - jnp.sum(grads * (moved - offset_float), axis=0)

    def warp(iteration):
        offset = shifts[iteration, :, 0, 0, 0]
        starts = [DMAX + offset[0], DMAX + offset[1], DMAX + offset[2]]
        return lax.dynamic_slice(deformed_ext, starts, (z_count, x_count, y_count)), offset

    def operator(delta):
        inner = jnp.sum(grads * interpolate(delta, tables, weights), axis=0)
        return share(restrict(grads * inner[None], tables, weights))

    warped, offset = warp(0)
    resid = image - warped + jnp.sum(grads * offset.astype(jnp.float32)[:, None, None, None], axis=0)
    products = jnp.stack([grads[i] * grads[j] for i, j in pairs])
    first = jnp.concatenate(
        [restrict(products, tables_sq, weights_sq), restrict(grads * resid[None], tables, weights)],
        axis=0,
    )
    first = share(first)
    diag = first[:6] + REGULARIZE * jnp.array([1.0, 1.0, 1.0, 0.0, 0.0, 0.0], jnp.float32)[
        :, None, None, None
    ]
    inverse = invert(diag)
    rhs = first[6:]
    nodal = jnp.zeros((3, z_count // ELEMENT + 1, x_count // ELEMENT + 1, y_count // ELEMENT + 1), jnp.float32)
    for iteration in range(ITERS):
        if iteration > 0:
            warped, offset = warp(iteration)
            resid = residual(interpolate(nodal, tables, weights), warped, offset)
            rhs = share(restrict(grads * resid[None], tables, weights))
        delta = DAMPING * apply_inverse(inverse, rhs)
        for sweep in range(SWEEPS - 1):
            applied = operator(delta) + REGULARIZE * delta
            delta = delta + DAMPING * apply_inverse(inverse, rhs - applied)
        nodal = nodal + delta
    final = residual(interpolate(nodal, tables, weights), warped, offset)
    return (nodal, final)


def solution(mesh):
    return jax.shard_map(
        shards,
        mesh=mesh,
        in_specs=(
            P(("gz", "gx"), None, "gy"),
            P(("gz", "gx"), None, "gy"),
            P(None, None, "gz", "gx", "gy"),
        ),
        out_specs=(P(None, "gz", "gx", "gy"), P("gz", "gx", "gy")),
        check_vma=False,
    )
```

```python
import numpy as np

import jax
import jax.numpy as jnp
from jax import lax
from jax.sharding import PartitionSpec as P

ELEMENT = 8
DMAX = 8
ITERS = 2
SWEEPS = 3


DAMPING = 0.7
REGULARIZE = 4.0
HI = lax.Precision.HIGHEST


def shape_table(voxel_count, squared=False):
    voxel = np.arange(voxel_count)
    fraction = ((voxel % ELEMENT).astype(np.float32) + 0.5) / ELEMENT
    owning = voxel // ELEMENT
    nodes = np.arange(voxel_count // ELEMENT + 1)
    lower = (nodes[None, :] == owning[:, None]) * (1.0 - fraction)[:, None]
    upper = (nodes[None, :] == owning[:, None] + 1) * fraction[:, None]
    table = (lower + upper).astype(np.float32)
    if squared:
        table = table * table
    return jnp.asarray(table)


def z_weights(squared=False):
    fraction = (np.arange(ELEMENT, dtype=np.float32) + 0.5) / ELEMENT
    lower = 1.0 - fraction
    if squared:
        return lower * lower, fraction * fraction
    return lower, fraction


def neighbours(axis):
    count = lax.axis_size(axis)
    forward = [(i, i + 1) for i in range(count - 1)]
    backward = [(i + 1, i) for i in range(count - 1)]
    return forward, backward


def halo(block, axis, dim, width):
    forward, backward = neighbours(axis)
    size = block.shape[dim]
    low = lax.ppermute(lax.slice_in_dim(block, size - width, size, axis=dim), axis, forward)
    high = lax.ppermute(lax.slice_in_dim(block, 0, width, axis=dim), axis, backward)
    return jnp.concatenate([low, block, high], axis=dim)


def share(partial_value):
    value = partial_value
    for axis, dim in (("gz", 1), ("gx", 2), ("gy", 3)):
        forward, backward = neighbours(axis)
        size = value.shape[dim]
        first = lax.slice_in_dim(value, 0, 1, axis=dim)
        last = lax.slice_in_dim(value, size - 1, size, axis=dim)
        from_low = lax.ppermute(last, axis, forward)
        from_high = lax.ppermute(first, axis, backward)
        middle = lax.slice_in_dim(value, 1, size - 1, axis=dim)
        value = jnp.concatenate([first + from_low, middle, last + from_high], axis=dim)
    return value


def cut_range(array, axis, start, length):
    return lax.slice_in_dim(array, start, start + length, axis=axis)


def smooth(array, axis):
    length = array.shape[axis] - 2
    return (
        cut_range(array, axis, 0, length)
        + 2.0 * cut_range(array, axis, 1, length)
        + cut_range(array, axis, 2, length)
    ) * 0.25


def differ(array, axis):
    length = array.shape[axis] - 2
    return (cut_range(array, axis, 2, length) - cut_range(array, axis, 0, length)) * 0.5


def gradients(extended):
    along_z = smooth(smooth(differ(extended, 0), 1), 2)
    along_x = smooth(smooth(differ(extended, 1), 0), 2)
    along_y = smooth(smooth(differ(extended, 2), 0), 1)
    return jnp.stack([along_z, along_x, along_y])


def interp_xy(nodal, table_x, table_y):
    step = jnp.einsum("cabd,yd->caby", nodal, table_y, precision=HI)
    return jnp.einsum("caby,xb->caxy", step, table_x, precision=HI)


def expand_z(values, weights):
    lower, upper = weights
    count = values.shape[1] - 1
    low = values[:, :count, None]
    high = values[:, 1:, None]
    shape = (1, 1, ELEMENT, 1, 1)
    joined = low * lower.reshape(shape) + high * upper.reshape(shape)
    return joined.reshape((values.shape[0], count * ELEMENT) + values.shape[2:])


def interpolate(nodal, tables, weights):
    return expand_z(interp_xy(nodal, *tables), weights)


def reduce_z(field, weights):
    lower, upper = weights
    count = field.shape[1] // ELEMENT
    blocks = field.reshape((field.shape[0], count, ELEMENT) + field.shape[2:])
    shape = (1, 1, ELEMENT, 1, 1)
    low = jnp.sum(blocks * lower.reshape(shape), axis=2)
    high = jnp.sum(blocks * upper.reshape(shape), axis=2)
    parts = [low[:, :1]]
    for e in range(1, count):
        parts.append(high[:, e - 1 : e] + low[:, e : e + 1])
    parts.append(high[:, count - 1 :])
    return jnp.concatenate(parts, axis=1)


def restrict(field, tables, weights):
    table_x, table_y = tables
    step = reduce_z(field, weights)
    step = jnp.einsum("caxy,xb->caby", step, table_x, precision=HI)
    return jnp.einsum("caby,yd->cabd", step, table_y, precision=HI)


def invert(diag):
    a, b, c, d, e, f = (diag[0], diag[1], diag[2], diag[3], diag[4], diag[5])
    i00 = b * c - f * f
    i11 = a * c - e * e
    i22 = a * b - d * d
    i01 = e * f - d * c
    i02 = d * f - b * e
    i12 = d * e - a * f
    det = a * i00 + d * i01 + e * i02
    return jnp.stack([i00, i11, i22, i01, i02, i12]) / det


def apply_inverse(inverse, vector):
    out_z = inverse[0] * vector[0] + inverse[3] * vector[1] + inverse[4] * vector[2]
    out_x = inverse[3] * vector[0] + inverse[1] * vector[1] + inverse[5] * vector[2]
    out_y = inverse[4] * vector[0] + inverse[5] * vector[1] + inverse[2] * vector[2]
    return jnp.stack([out_z, out_x, out_y])


def bricks_of(image_slab, deformed_slab):
    image = lax.all_to_all(image_slab, "gx", split_axis=1, concat_axis=0, tiled=True)
    deformed = lax.all_to_all(deformed_slab, "gx", split_axis=1, concat_axis=0, tiled=True)
    both = jnp.stack([image, deformed])
    both = halo(both, "gy", 3, DMAX)
    both = halo(both, "gx", 2, DMAX)
    forward, backward = neighbours("gz")
    bz, nx, ny = both.shape[1:]
    image = both[0]
    deformed = both[1]
    to_high = jnp.concatenate([deformed[bz - DMAX :], image[bz - 1 :]], axis=0)
    to_low = jnp.concatenate([deformed[:DMAX], image[:1]], axis=0)
    from_low = lax.ppermute(to_high, "gz", forward)
    from_high = lax.ppermute(to_low, "gz", backward)
    deformed_ext = jnp.concatenate([from_low[:DMAX], deformed, from_high[:DMAX]], axis=0)
    image_ext = jnp.concatenate([from_low[DMAX:], image, from_high[DMAX:]], axis=0)
    image_ext = image_ext[:, DMAX - 1 : nx - DMAX + 1, DMAX - 1 : ny - DMAX + 1]
    return image_ext, deformed_ext


def shards(image_slab, deformed_slab, shifts):
    image_ext, deformed_ext = bricks_of(image_slab, deformed_slab)
    image = image_ext[1:-1, 1:-1, 1:-1]
    z_count, x_count, y_count = image.shape
    grads = gradients(image_ext)
    tables = (shape_table(x_count), shape_table(y_count))
    tables_sq = (shape_table(x_count, True), shape_table(y_count, True))
    weights = z_weights(False)
    weights_sq = z_weights(True)
    pairs = ((0, 0), (1, 1), (2, 2), (0, 1), (0, 2), (1, 2))

    def residual(moved, warped_now, offset):
        offset_float = offset.astype(jnp.float32)[:, None, None, None]
        return image - warped_now - jnp.sum(grads * (moved - offset_float), axis=0)

    def warp(iteration):
        offset = shifts[iteration, :, 0, 0, 0]
        starts = [DMAX + offset[0], DMAX + offset[1], DMAX + offset[2]]
        return lax.dynamic_slice(deformed_ext, starts, (z_count, x_count, y_count)), offset

    def operator(delta):
        inner = jnp.sum(grads * interpolate(delta, tables, weights), axis=0)
        return share(restrict(grads * inner[None], tables, weights))

    warped, offset = warp(0)
    resid = image - warped + jnp.sum(grads * offset.astype(jnp.float32)[:, None, None, None], axis=0)
    products = jnp.stack([grads[i] * grads[j] for i, j in pairs])
    first = jnp.concatenate(
        [restrict(products, tables_sq, weights_sq), restrict(grads * resid[None], tables, weights)],
        axis=0,
    )
    first = share(first)
    diag = first[:6] + REGULARIZE * jnp.array([1.0, 1.0, 1.0, 0.0, 0.0, 0.0], jnp.float32)[
        :, None, None, None
    ]
    inverse = invert(diag)
    rhs = first[6:]
    nodal = jnp.zeros((3, z_count // ELEMENT + 1, x_count // ELEMENT + 1, y_count // ELEMENT + 1), jnp.float32)
    for iteration in range(ITERS):
        if iteration > 0:
            warped, offset = warp(iteration)
            resid = residual(interpolate(nodal, tables, weights), warped, offset)
            rhs = share(restrict(grads * resid[None], tables, weights))
        delta = DAMPING * apply_inverse(inverse, rhs)
        for sweep in range(SWEEPS - 1):
            applied = operator(delta) + REGULARIZE * delta
            delta = delta + DAMPING * apply_inverse(inverse, rhs - applied)
        nodal = nodal + delta
    final = residual(interpolate(nodal, tables, weights), warped, offset)
    return (nodal, final)


def solution(mesh):
    return jax.shard_map(
        shards,
        mesh=mesh,
        in_specs=(
            P(("gz", "gx"), None, "gy"),
            P(("gz", "gx"), None, "gy"),
            P(None, None, "gz", "gx", "gy"),
        ),
        out_specs=(P(None, "gz", "gx", "gy"), P("gz", "gx", "gy")),
        check_vma=False,
    )
```

```python
import numpy as np

import jax
import jax.numpy as jnp
from jax import lax
from jax.sharding import PartitionSpec as P

ELEMENT = 8
DMAX = 8
ITERS = 2
SWEEPS = 3


DAMPING = 0.7
REGULARIZE = 4.0
HI = lax.Precision.HIGHEST


def shape_table(voxel_count, squared=False):
    voxel = np.arange(voxel_count)
    fraction = ((voxel % ELEMENT).astype(np.float32) + 0.5) / ELEMENT
    owning = voxel // ELEMENT
    nodes = np.arange(voxel_count // ELEMENT + 1)
    lower = (nodes[None, :] == owning[:, None]) * (1.0 - fraction)[:, None]
    upper = (nodes[None, :] == owning[:, None] + 1) * fraction[:, None]
    table = (lower + upper).astype(np.float32)
    if squared:
        table = table * table
    return jnp.asarray(table)


def z_weights(squared=False):
    fraction = (np.arange(ELEMENT, dtype=np.float32) + 0.5) / ELEMENT
    lower = 1.0 - fraction
    if squared:
        return lower * lower, fraction * fraction
    return lower, fraction


def neighbours(axis):
    count = lax.axis_size(axis)
    forward = [(i, i + 1) for i in range(count - 1)]
    backward = [(i + 1, i) for i in range(count - 1)]
    return forward, backward


def halo(block, axis, dim, width):
    forward, backward = neighbours(axis)
    size = block.shape[dim]
    low = lax.ppermute(lax.slice_in_dim(block, size - width, size, axis=dim), axis, forward)
    high = lax.ppermute(lax.slice_in_dim(block, 0, width, axis=dim), axis, backward)
    return jnp.concatenate([low, block, high], axis=dim)


def share(partial_value):
    value = partial_value
    for axis, dim in (("gz", 1), ("gx", 2), ("gy", 3)):
        forward, backward = neighbours(axis)
        size = value.shape[dim]
        first = lax.slice_in_dim(value, 0, 1, axis=dim)
        last = lax.slice_in_dim(value, size - 1, size, axis=dim)
        from_low = lax.ppermute(last, axis, forward)
        from_high = lax.ppermute(first, axis, backward)
        middle = lax.slice_in_dim(value, 1, size - 1, axis=dim)
        value = jnp.concatenate([first + from_low, middle, last + from_high], axis=dim)
    return value


def cut_range(array, axis, start, length):
    return lax.slice_in_dim(array, start, start + length, axis=axis)


def smooth(array, axis):
    length = array.shape[axis] - 2
    return (
        cut_range(array, axis, 0, length)
        + 2.0 * cut_range(array, axis, 1, length)
        + cut_range(array, axis, 2, length)
    ) * 0.25


def differ(array, axis):
    length = array.shape[axis] - 2
    return (cut_range(array, axis, 2, length) - cut_range(array, axis, 0, length)) * 0.5


def gradients(extended):
    along_z = smooth(smooth(differ(extended, 0), 1), 2)
    along_x = smooth(smooth(differ(extended, 1), 0), 2)
    along_y = smooth(smooth(differ(extended, 2), 0), 1)
    return jnp.stack([along_z, along_x, along_y])


def interp_xy(nodal, table_x, table_y):
    step = jnp.einsum("cabd,yd->caby", nodal, table_y, precision=HI)
    return jnp.einsum("caby,xb->caxy", step, table_x, precision=HI)


def expand_z(values, weights):
    lower, upper = weights
    count = values.shape[1] - 1
    low = values[:, :count, None]
    high = values[:, 1:, None]
    shape = (1, 1, ELEMENT, 1, 1)
    joined = low * lower.reshape(shape) + high * upper.reshape(shape)
    return joined.reshape((values.shape[0], count * ELEMENT) + values.shape[2:])


def interpolate(nodal, tables, weights):
    return expand_z(interp_xy(nodal, *tables), weights)


def reduce_z(field, weights):
    lower, upper = weights
    count = field.shape[1] // ELEMENT
    blocks = field.reshape((field.shape[0], count, ELEMENT) + field.shape[2:])
    shape = (1, 1, ELEMENT, 1, 1)
    low = jnp.sum(blocks * lower.reshape(shape), axis=2)
    high = jnp.sum(blocks * upper.reshape(shape), axis=2)
    parts = [low[:, :1]]
    for e in range(1, count):
        parts.append(high[:, e - 1 : e] + low[:, e : e + 1])
    parts.append(high[:, count - 1 :])
    return jnp.concatenate(parts, axis=1)


def restrict(field, tables, weights):
    table_x, table_y = tables
    step = reduce_z(field, weights)
    step = jnp.einsum("caxy,xb->caby", step, table_x, precision=HI)
    return jnp.einsum("caby,yd->cabd", step, table_y, precision=HI)


def invert(diag):
    a, b, c, d, e, f = (diag[0], diag[1], diag[2], diag[3], diag[4], diag[5])
    i00 = b * c - f * f
    i11 = a * c - e * e
    i22 = a * b - d * d
    i01 = e * f - d * c
    i02 = d * f - b * e
    i12 = d * e - a * f
    det = a * i00 + d * i01 + e * i02
    return jnp.stack([i00, i11, i22, i01, i02, i12]) / det


def apply_inverse(inverse, vector):
    out_z = inverse[0] * vector[0] + inverse[3] * vector[1] + inverse[4] * vector[2]
    out_x = inverse[3] * vector[0] + inverse[1] * vector[1] + inverse[5] * vector[2]
    out_y = inverse[4] * vector[0] + inverse[5] * vector[1] + inverse[2] * vector[2]
    return jnp.stack([out_z, out_x, out_y])


def bricks_of(image_slab, deformed_slab):
    both = jnp.concatenate([image_slab, deformed_slab], axis=0)
    both = halo(both, "gy", 2, DMAX)
    n_gx = lax.axis_size("gx")
    fields, nx, ny = both.shape
    bx = nx // n_gx
    main = both.reshape(fields, n_gx, bx, ny)
    zero = jnp.zeros((fields, 1, DMAX, ny), both.dtype)
    low = jnp.concatenate([zero, main[:, :-1, bx - DMAX :]], axis=1)
    high = jnp.concatenate([main[:, 1:, :DMAX], zero], axis=1)
    windows = jnp.concatenate([low, main, high], axis=2)
    windows = jnp.moveaxis(windows, 1, 0)
    width = bx + 2 * DMAX
    lanes = 128 if (width * ny) % 128 == 0 else ny
    packed = windows.reshape(n_gx, fields, width * ny // lanes, lanes)
    brick = lax.all_to_all(packed, "gx", split_axis=0, concat_axis=0, tiled=True)
    brick = brick.reshape(n_gx, fields, width, ny)
    image = brick[:, 0]
    deformed = brick[:, 1]
    image_ext = halo(image[:, DMAX - 1 : DMAX + bx + 1, DMAX - 1 : ny - DMAX + 1], "gz", 0, 1)
    deformed_ext = halo(deformed, "gz", 0, DMAX)
    return image_ext, deformed_ext


def shards(image_slab, deformed_slab, shifts):
    image_ext, deformed_ext = bricks_of(image_slab, deformed_slab)
    image = image_ext[1:-1, 1:-1, 1:-1]
    z_count, x_count, y_count = image.shape
    grads = gradients(image_ext)
    tables = (shape_table(x_count), shape_table(y_count))
    tables_sq = (shape_table(x_count, True), shape_table(y_count, True))
    weights = z_weights(False)
    weights_sq = z_weights(True)
    pairs = ((0, 0), (1, 1), (2, 2), (0, 1), (0, 2), (1, 2))

    def residual(moved, warped_now, offset):
        offset_float = offset.astype(jnp.float32)[:, None, None, None]
        return image - warped_now - jnp.sum(grads * (moved - offset_float), axis=0)

    def warp(iteration):
        offset = shifts[iteration, :, 0, 0, 0]
        starts = [DMAX + offset[0], DMAX + offset[1], DMAX + offset[2]]
        return lax.dynamic_slice(deformed_ext, starts, (z_count, x_count, y_count)), offset

    def operator(delta):
        inner = jnp.sum(grads * interpolate(delta, tables, weights), axis=0)
        return share(restrict(grads * inner[None], tables, weights))

    warped, offset = warp(0)
    resid = image - warped + jnp.sum(grads * offset.astype(jnp.float32)[:, None, None, None], axis=0)
    products = jnp.stack([grads[i] * grads[j] for i, j in pairs])
    first = jnp.concatenate(
        [restrict(products, tables_sq, weights_sq), restrict(grads * resid[None], tables, weights)],
        axis=0,
    )
    first = share(first)
    diag = first[:6] + REGULARIZE * jnp.array([1.0, 1.0, 1.0, 0.0, 0.0, 0.0], jnp.float32)[
        :, None, None, None
    ]
    inverse = invert(diag)
    rhs = first[6:]
    nodal = jnp.zeros((3, z_count // ELEMENT + 1, x_count // ELEMENT + 1, y_count // ELEMENT + 1), jnp.float32)
    for iteration in range(ITERS):
        if iteration > 0:
            warped, offset = warp(iteration)
            resid = residual(interpolate(nodal, tables, weights), warped, offset)
            rhs = share(restrict(grads * resid[None], tables, weights))
        delta = DAMPING * apply_inverse(inverse, rhs)
        for sweep in range(SWEEPS - 1):
            applied = operator(delta) + REGULARIZE * delta
            delta = delta + DAMPING * apply_inverse(inverse, rhs - applied)
        nodal = nodal + delta
    final = residual(interpolate(nodal, tables, weights), warped, offset)
    return (nodal, final)


def solution(mesh):
    return jax.shard_map(
        shards,
        mesh=mesh,
        in_specs=(
            P(("gz", "gx"), None, "gy"),
            P(("gz", "gx"), None, "gy"),
            P(None, None, "gz", "gx", "gy"),
        ),
        out_specs=(P(None, "gz", "gx", "gy"), P("gz", "gx", "gy")),
        check_vma=False,
    )
```

```python
import numpy as np

import jax
import jax.numpy as jnp
from jax import lax
from jax.sharding import PartitionSpec as P

ELEMENT = 8
DMAX = 8
ITERS = 2
SWEEPS = 3


DAMPING = 0.7
REGULARIZE = 4.0
HI = lax.Precision.HIGHEST


def shape_table(voxel_count, squared=False):
    voxel = np.arange(voxel_count)
    fraction = ((voxel % ELEMENT).astype(np.float32) + 0.5) / ELEMENT
    owning = voxel // ELEMENT
    nodes = np.arange(voxel_count // ELEMENT + 1)
    lower = (nodes[None, :] == owning[:, None]) * (1.0 - fraction)[:, None]
    upper = (nodes[None, :] == owning[:, None] + 1) * fraction[:, None]
    table = (lower + upper).astype(np.float32)
    if squared:
        table = table * table
    return jnp.asarray(table)


def z_weights(squared=False):
    fraction = (np.arange(ELEMENT, dtype=np.float32) + 0.5) / ELEMENT
    lower = 1.0 - fraction
    if squared:
        return lower * lower, fraction * fraction
    return lower, fraction


def neighbours(axis):
    count = lax.axis_size(axis)
    forward = [(i, i + 1) for i in range(count - 1)]
    backward = [(i + 1, i) for i in range(count - 1)]
    return forward, backward


def halo(block, axis, dim, width):
    forward, backward = neighbours(axis)
    size = block.shape[dim]
    low = lax.ppermute(lax.slice_in_dim(block, size - width, size, axis=dim), axis, forward)
    high = lax.ppermute(lax.slice_in_dim(block, 0, width, axis=dim), axis, backward)
    return jnp.concatenate([low, block, high], axis=dim)


def share(partial_value):
    value = partial_value
    for axis, dim in (("gz", 1), ("gx", 2), ("gy", 3)):
        forward, backward = neighbours(axis)
        size = value.shape[dim]
        first = lax.slice_in_dim(value, 0, 1, axis=dim)
        last = lax.slice_in_dim(value, size - 1, size, axis=dim)
        from_low = lax.ppermute(last, axis, forward)
        from_high = lax.ppermute(first, axis, backward)
        middle = lax.slice_in_dim(value, 1, size - 1, axis=dim)
        value = jnp.concatenate([first + from_low, middle, last + from_high], axis=dim)
    return value


def cut_range(array, axis, start, length):
    return lax.slice_in_dim(array, start, start + length, axis=axis)


def smooth(array, axis):
    length = array.shape[axis] - 2
    return (
        cut_range(array, axis, 0, length)
        + 2.0 * cut_range(array, axis, 1, length)
        + cut_range(array, axis, 2, length)
    ) * 0.25


def differ(array, axis):
    length = array.shape[axis] - 2
    return (cut_range(array, axis, 2, length) - cut_range(array, axis, 0, length)) * 0.5


def gradients(extended):
    along_z = smooth(smooth(differ(extended, 0), 1), 2)
    along_x = smooth(smooth(differ(extended, 1), 0), 2)
    along_y = smooth(smooth(differ(extended, 2), 0), 1)
    return jnp.stack([along_z, along_x, along_y])


def interp_xy(nodal, table_x, table_y):
    step = jnp.einsum("cabd,yd->caby", nodal, table_y, precision=HI)
    return jnp.einsum("caby,xb->caxy", step, table_x, precision=HI)


def expand_z(values, weights):
    lower, upper = weights
    count = values.shape[1] - 1
    low = values[:, :count, None]
    high = values[:, 1:, None]
    shape = (1, 1, ELEMENT, 1, 1)
    joined = low * lower.reshape(shape) + high * upper.reshape(shape)
    return joined.reshape((values.shape[0], count * ELEMENT) + values.shape[2:])


def interpolate(nodal, tables, weights):
    return expand_z(interp_xy(nodal, *tables), weights)


def reduce_z(field, weights):
    lower, upper = weights
    count = field.shape[1] // ELEMENT
    blocks = field.reshape((field.shape[0], count, ELEMENT) + field.shape[2:])
    shape = (1, 1, ELEMENT, 1, 1)
    low = jnp.sum(blocks * lower.reshape(shape), axis=2)
    high = jnp.sum(blocks * upper.reshape(shape), axis=2)
    parts = [low[:, :1]]
    for e in range(1, count):
        parts.append(high[:, e - 1 : e] + low[:, e : e + 1])
    parts.append(high[:, count - 1 :])
    return jnp.concatenate(parts, axis=1)


def restrict(field, tables, weights):
    table_x, table_y = tables
    step = reduce_z(field, weights)
    step = jnp.einsum("caxy,xb->caby", step, table_x, precision=HI)
    return jnp.einsum("caby,yd->cabd", step, table_y, precision=HI)


def invert(diag):
    a, b, c, d, e, f = (diag[0], diag[1], diag[2], diag[3], diag[4], diag[5])
    i00 = b * c - f * f
    i11 = a * c - e * e
    i22 = a * b - d * d
    i01 = e * f - d * c
    i02 = d * f - b * e
    i12 = d * e - a * f
    det = a * i00 + d * i01 + e * i02
    return jnp.stack([i00, i11, i22, i01, i02, i12]) / det


def apply_inverse(inverse, vector):
    out_z = inverse[0] * vector[0] + inverse[3] * vector[1] + inverse[4] * vector[2]
    out_x = inverse[3] * vector[0] + inverse[1] * vector[1] + inverse[5] * vector[2]
    out_y = inverse[4] * vector[0] + inverse[5] * vector[1] + inverse[2] * vector[2]
    return jnp.stack([out_z, out_x, out_y])


def bricks_of(image_slab, deformed_slab):
    both = jnp.concatenate([image_slab, deformed_slab], axis=0)
    both = halo(both, "gy", 2, DMAX)
    n_gx = lax.axis_size("gx")
    fields, nx, ny = both.shape
    bx = nx // n_gx
    main = both.reshape(fields, n_gx, bx, ny)
    zero = jnp.zeros((fields, 1, DMAX, ny), both.dtype)
    low = jnp.concatenate([zero, main[:, :-1, bx - DMAX :]], axis=1)
    high = jnp.concatenate([main[:, 1:, :DMAX], zero], axis=1)
    windows = jnp.concatenate([low, main, high], axis=2)
    windows = jnp.moveaxis(windows, 1, 0)
    brick = lax.all_to_all(windows, "gx", split_axis=0, concat_axis=0, tiled=True)
    image = brick[:, 0]
    deformed = brick[:, 1]
    image_ext = halo(image[:, DMAX - 1 : DMAX + bx + 1, DMAX - 1 : ny - DMAX + 1], "gz", 0, 1)
    deformed_ext = halo(deformed, "gz", 0, DMAX)
    return image_ext, deformed_ext


def shards(image_slab, deformed_slab, shifts):
    image_ext, deformed_ext = bricks_of(image_slab, deformed_slab)
    image = image_ext[1:-1, 1:-1, 1:-1]
    z_count, x_count, y_count = image.shape
    grads = gradients(image_ext)
    tables = (shape_table(x_count), shape_table(y_count))
    tables_sq = (shape_table(x_count, True), shape_table(y_count, True))
    weights = z_weights(False)
    weights_sq = z_weights(True)
    pairs = ((0, 0), (1, 1), (2, 2), (0, 1), (0, 2), (1, 2))

    def residual(moved, warped_now, offset):
        offset_float = offset.astype(jnp.float32)[:, None, None, None]
        return image - warped_now - jnp.sum(grads * (moved - offset_float), axis=0)

    def warp(iteration):
        offset = shifts[iteration, :, 0, 0, 0]
        starts = [DMAX + offset[0], DMAX + offset[1], DMAX + offset[2]]
        return lax.dynamic_slice(deformed_ext, starts, (z_count, x_count, y_count)), offset

    def operator(delta):
        inner = jnp.sum(grads * interpolate(delta, tables, weights), axis=0)
        return share(restrict(grads * inner[None], tables, weights))

    warped, offset = warp(0)
    resid = image - warped + jnp.sum(grads * offset.astype(jnp.float32)[:, None, None, None], axis=0)
    products = jnp.stack([grads[i] * grads[j] for i, j in pairs])
    first = jnp.concatenate(
        [restrict(products, tables_sq, weights_sq), restrict(grads * resid[None], tables, weights)],
        axis=0,
    )
    first = share(first)
    diag = first[:6] + REGULARIZE * jnp.array([1.0, 1.0, 1.0, 0.0, 0.0, 0.0], jnp.float32)[
        :, None, None, None
    ]
    inverse = invert(diag)
    rhs = first[6:]
    nodal = jnp.zeros((3, z_count // ELEMENT + 1, x_count // ELEMENT + 1, y_count // ELEMENT + 1), jnp.float32)
    for iteration in range(ITERS):
        if iteration > 0:
            warped, offset = warp(iteration)
            resid = residual(interpolate(nodal, tables, weights), warped, offset)
            rhs = share(restrict(grads * resid[None], tables, weights))
        delta = DAMPING * apply_inverse(inverse, rhs)

        def sweep(_, delta, rhs=rhs):
            applied = operator(delta) + REGULARIZE * delta
            return delta + DAMPING * apply_inverse(inverse, rhs - applied)

        delta = lax.fori_loop(0, SWEEPS - 1, sweep, delta)
        nodal = nodal + delta
    final = residual(interpolate(nodal, tables, weights), warped, offset)
    return (nodal, final)


def solution(mesh):
    return jax.shard_map(
        shards,
        mesh=mesh,
        in_specs=(
            P(("gz", "gx"), None, "gy"),
            P(("gz", "gx"), None, "gy"),
            P(None, None, "gz", "gx", "gy"),
        ),
        out_specs=(P(None, "gz", "gx", "gy"), P("gz", "gx", "gy")),
        check_vma=False,
    )
```

```python
import numpy as np

import jax
import jax.numpy as jnp
from jax import lax
from jax.sharding import PartitionSpec as P

ELEMENT = 8
DMAX = 8
ITERS = 2
SWEEPS = 3


DAMPING = 0.7
REGULARIZE = 4.0
HI = lax.Precision.HIGHEST


def shape_table(voxel_count, squared=False):
    voxel = np.arange(voxel_count)
    fraction = ((voxel % ELEMENT).astype(np.float32) + 0.5) / ELEMENT
    owning = voxel // ELEMENT
    nodes = np.arange(voxel_count // ELEMENT + 1)
    lower = (nodes[None, :] == owning[:, None]) * (1.0 - fraction)[:, None]
    upper = (nodes[None, :] == owning[:, None] + 1) * fraction[:, None]
    table = (lower + upper).astype(np.float32)
    if squared:
        table = table * table
    return jnp.asarray(table)


def z_weights(squared=False):
    fraction = (np.arange(ELEMENT, dtype=np.float32) + 0.5) / ELEMENT
    lower = 1.0 - fraction
    if squared:
        return lower * lower, fraction * fraction
    return lower, fraction


def neighbours(axis):
    count = lax.axis_size(axis)
    forward = [(i, i + 1) for i in range(count - 1)]
    backward = [(i + 1, i) for i in range(count - 1)]
    return forward, backward


def halo(block, axis, dim, width):
    forward, backward = neighbours(axis)
    size = block.shape[dim]
    low = lax.ppermute(lax.slice_in_dim(block, size - width, size, axis=dim), axis, forward)
    high = lax.ppermute(lax.slice_in_dim(block, 0, width, axis=dim), axis, backward)
    return jnp.concatenate([low, block, high], axis=dim)


def share(partial_value):
    value = partial_value
    for axis, dim in (("gz", 1), ("gx", 2), ("gy", 3)):
        forward, backward = neighbours(axis)
        size = value.shape[dim]
        first = lax.slice_in_dim(value, 0, 1, axis=dim)
        last = lax.slice_in_dim(value, size - 1, size, axis=dim)
        from_low = lax.ppermute(last, axis, forward)
        from_high = lax.ppermute(first, axis, backward)
        middle = lax.slice_in_dim(value, 1, size - 1, axis=dim)
        value = jnp.concatenate([first + from_low, middle, last + from_high], axis=dim)
    return value


def cut_range(array, axis, start, length):
    return lax.slice_in_dim(array, start, start + length, axis=axis)


def smooth(array, axis):
    length = array.shape[axis] - 2
    return (
        cut_range(array, axis, 0, length)
        + 2.0 * cut_range(array, axis, 1, length)
        + cut_range(array, axis, 2, length)
    ) * 0.25


def differ(array, axis):
    length = array.shape[axis] - 2
    return (cut_range(array, axis, 2, length) - cut_range(array, axis, 0, length)) * 0.5


def gradients(extended):
    along_z = smooth(smooth(differ(extended, 0), 1), 2)
    along_x = smooth(smooth(differ(extended, 1), 0), 2)
    along_y = smooth(smooth(differ(extended, 2), 0), 1)
    return jnp.stack([along_z, along_x, along_y])


def interp_xy(nodal, table_x, table_y):
    step = jnp.einsum("cabd,yd->caby", nodal, table_y, precision=HI)
    return jnp.einsum("caby,xb->caxy", step, table_x, precision=HI)


def expand_z(values, weights):
    lower, upper = weights
    count = values.shape[1] - 1
    low = values[:, :count, None]
    high = values[:, 1:, None]
    shape = (1, 1, ELEMENT, 1, 1)
    joined = low * lower.reshape(shape) + high * upper.reshape(shape)
    return joined.reshape((values.shape[0], count * ELEMENT) + values.shape[2:])


def interpolate(nodal, tables, weights):
    return expand_z(interp_xy(nodal, *tables), weights)


def reduce_z(field, weights):
    lower, upper = weights
    count = field.shape[1] // ELEMENT
    blocks = field.reshape((field.shape[0], count, ELEMENT) + field.shape[2:])
    shape = (1, 1, ELEMENT, 1, 1)
    low = jnp.sum(blocks * lower.reshape(shape), axis=2)
    high = jnp.sum(blocks * upper.reshape(shape), axis=2)
    parts = [low[:, :1]]
    for e in range(1, count):
        parts.append(high[:, e - 1 : e] + low[:, e : e + 1])
    parts.append(high[:, count - 1 :])
    return jnp.concatenate(parts, axis=1)


def restrict(field, tables, weights):
    table_x, table_y = tables
    step = reduce_z(field, weights)
    step = jnp.einsum("caxy,xb->caby", step, table_x, precision=HI)
    return jnp.einsum("caby,yd->cabd", step, table_y, precision=HI)


def invert(diag):
    a, b, c, d, e, f = (diag[0], diag[1], diag[2], diag[3], diag[4], diag[5])
    i00 = b * c - f * f
    i11 = a * c - e * e
    i22 = a * b - d * d
    i01 = e * f - d * c
    i02 = d * f - b * e
    i12 = d * e - a * f
    det = a * i00 + d * i01 + e * i02
    return jnp.stack([i00, i11, i22, i01, i02, i12]) / det


def apply_inverse(inverse, vector):
    out_z = inverse[0] * vector[0] + inverse[3] * vector[1] + inverse[4] * vector[2]
    out_x = inverse[3] * vector[0] + inverse[1] * vector[1] + inverse[5] * vector[2]
    out_y = inverse[4] * vector[0] + inverse[5] * vector[1] + inverse[2] * vector[2]
    return jnp.stack([out_z, out_x, out_y])


def bricks_of(image_slab, deformed_slab):
    both = jnp.concatenate([image_slab, deformed_slab], axis=0)
    n_gx = lax.axis_size("gx")
    fields, nx, ny = both.shape
    bx = nx // n_gx
    main = both.reshape(fields, n_gx, bx, ny)
    zero = jnp.zeros((fields, 1, DMAX, ny), both.dtype)
    low = jnp.concatenate([zero, main[:, :-1, bx - DMAX :]], axis=1)
    high = jnp.concatenate([main[:, 1:, :DMAX], zero], axis=1)
    windows = jnp.concatenate([low, main, high], axis=2)
    windows = jnp.moveaxis(windows, 1, 0)
    brick = lax.all_to_all(windows, "gx", split_axis=0, concat_axis=0, tiled=True)
    brick = halo(brick, "gy", 3, DMAX)
    ny = brick.shape[3]
    image = brick[:, 0]
    deformed = brick[:, 1]
    image_ext = halo(image[:, DMAX - 1 : DMAX + bx + 1, DMAX - 1 : ny - DMAX + 1], "gz", 0, 1)
    deformed_ext = halo(deformed, "gz", 0, DMAX)
    return image_ext, deformed_ext


def shards(image_slab, deformed_slab, shifts):
    image_ext, deformed_ext = bricks_of(image_slab, deformed_slab)
    image = image_ext[1:-1, 1:-1, 1:-1]
    z_count, x_count, y_count = image.shape
    grads = gradients(image_ext)
    tables = (shape_table(x_count), shape_table(y_count))
    tables_sq = (shape_table(x_count, True), shape_table(y_count, True))
    weights = z_weights(False)
    weights_sq = z_weights(True)
    pairs = ((0, 0), (1, 1), (2, 2), (0, 1), (0, 2), (1, 2))

    def residual(moved, warped_now, offset):
        offset_float = offset.astype(jnp.float32)[:, None, None, None]
        return image - warped_now - jnp.sum(grads * (moved - offset_float), axis=0)

    def warp(iteration):
        offset = shifts[iteration, :, 0, 0, 0]
        starts = [DMAX + offset[0], DMAX + offset[1], DMAX + offset[2]]
        return lax.dynamic_slice(deformed_ext, starts, (z_count, x_count, y_count)), offset

    def operator(delta):
        inner = jnp.sum(grads * interpolate(delta, tables, weights), axis=0)
        return share(restrict(grads * inner[None], tables, weights))

    warped, offset = warp(0)
    resid = image - warped + jnp.sum(grads * offset.astype(jnp.float32)[:, None, None, None], axis=0)
    products = jnp.stack([grads[i] * grads[j] for i, j in pairs])
    first = jnp.concatenate(
        [restrict(products, tables_sq, weights_sq), restrict(grads * resid[None], tables, weights)],
        axis=0,
    )
    first = share(first)
    diag = first[:6] + REGULARIZE * jnp.array([1.0, 1.0, 1.0, 0.0, 0.0, 0.0], jnp.float32)[
        :, None, None, None
    ]
    inverse = invert(diag)
    rhs = first[6:]
    nodal = jnp.zeros((3, z_count // ELEMENT + 1, x_count // ELEMENT + 1, y_count // ELEMENT + 1), jnp.float32)
    for iteration in range(ITERS):
        if iteration > 0:
            warped, offset = warp(iteration)
            resid = residual(interpolate(nodal, tables, weights), warped, offset)
            rhs = share(restrict(grads * resid[None], tables, weights))
        delta = DAMPING * apply_inverse(inverse, rhs)
        for sweep in range(SWEEPS - 1):
            applied = operator(delta) + REGULARIZE * delta
            delta = delta + DAMPING * apply_inverse(inverse, rhs - applied)
        nodal = nodal + delta
    final = residual(interpolate(nodal, tables, weights), warped, offset)
    return (nodal, final)


def solution(mesh):
    return jax.shard_map(
        shards,
        mesh=mesh,
        in_specs=(
            P(("gz", "gx"), None, "gy"),
            P(("gz", "gx"), None, "gy"),
            P(None, None, "gz", "gx", "gy"),
        ),
        out_specs=(P(None, "gz", "gx", "gy"), P("gz", "gx", "gy")),
        check_vma=False,
    )
```

```python
import numpy as np

import jax
import jax.numpy as jnp
from jax import lax
from jax.sharding import PartitionSpec as P

ELEMENT = 8
DMAX = 8
ITERS = 2
SWEEPS = 3


DAMPING = 0.7
REGULARIZE = 4.0
HI = lax.Precision.HIGHEST


def shape_table(voxel_count, squared=False):
    voxel = np.arange(voxel_count)
    fraction = ((voxel % ELEMENT).astype(np.float32) + 0.5) / ELEMENT
    owning = voxel // ELEMENT
    nodes = np.arange(voxel_count // ELEMENT + 1)
    lower = (nodes[None, :] == owning[:, None]) * (1.0 - fraction)[:, None]
    upper = (nodes[None, :] == owning[:, None] + 1) * fraction[:, None]
    table = (lower + upper).astype(np.float32)
    if squared:
        table = table * table
    return jnp.asarray(table)


def z_weights(squared=False):
    fraction = (np.arange(ELEMENT, dtype=np.float32) + 0.5) / ELEMENT
    lower = 1.0 - fraction
    if squared:
        return lower * lower, fraction * fraction
    return lower, fraction


def neighbours(axis):
    count = lax.axis_size(axis)
    forward = [(i, i + 1) for i in range(count - 1)]
    backward = [(i + 1, i) for i in range(count - 1)]
    return forward, backward


def halo(block, axis, dim, width):
    forward, backward = neighbours(axis)
    size = block.shape[dim]
    low = lax.ppermute(lax.slice_in_dim(block, size - width, size, axis=dim), axis, forward)
    high = lax.ppermute(lax.slice_in_dim(block, 0, width, axis=dim), axis, backward)
    return jnp.concatenate([low, block, high], axis=dim)


def share(partial_value):
    value = partial_value
    for axis, dim in (("gz", 1), ("gx", 2), ("gy", 3)):
        forward, backward = neighbours(axis)
        size = value.shape[dim]
        first = lax.slice_in_dim(value, 0, 1, axis=dim)
        last = lax.slice_in_dim(value, size - 1, size, axis=dim)
        from_low = lax.ppermute(last, axis, forward)
        from_high = lax.ppermute(first, axis, backward)
        middle = lax.slice_in_dim(value, 1, size - 1, axis=dim)
        value = jnp.concatenate([first + from_low, middle, last + from_high], axis=dim)
    return value


def cut_range(array, axis, start, length):
    return lax.slice_in_dim(array, start, start + length, axis=axis)


def smooth(array, axis):
    length = array.shape[axis] - 2
    return (
        cut_range(array, axis, 0, length)
        + 2.0 * cut_range(array, axis, 1, length)
        + cut_range(array, axis, 2, length)
    ) * 0.25


def differ(array, axis):
    length = array.shape[axis] - 2
    return (cut_range(array, axis, 2, length) - cut_range(array, axis, 0, length)) * 0.5


def gradients(extended):
    along_z = smooth(smooth(differ(extended, 0), 1), 2)
    along_x = smooth(smooth(differ(extended, 1), 0), 2)
    along_y = smooth(smooth(differ(extended, 2), 0), 1)
    return jnp.stack([along_z, along_x, along_y])


def interp_xy(nodal, table_x, table_y):
    step = jnp.einsum("cabd,yd->caby", nodal, table_y, precision=HI)
    return jnp.einsum("caby,xb->caxy", step, table_x, precision=HI)


def expand_z(values, weights):
    lower, upper = weights
    count = values.shape[1] - 1
    low = values[:, :count, None]
    high = values[:, 1:, None]
    shape = (1, 1, ELEMENT, 1, 1)
    joined = low * lower.reshape(shape) + high * upper.reshape(shape)
    return joined.reshape((values.shape[0], count * ELEMENT) + values.shape[2:])


def interpolate(nodal, tables, weights):
    return expand_z(interp_xy(nodal, *tables), weights)


def reduce_z(field, weights):
    lower, upper = weights
    count = field.shape[1] // ELEMENT
    blocks = field.reshape((field.shape[0], count, ELEMENT) + field.shape[2:])
    shape = (1, 1, ELEMENT, 1, 1)
    low = jnp.sum(blocks * lower.reshape(shape), axis=2)
    high = jnp.sum(blocks * upper.reshape(shape), axis=2)
    parts = [low[:, :1]]
    for e in range(1, count):
        parts.append(high[:, e - 1 : e] + low[:, e : e + 1])
    parts.append(high[:, count - 1 :])
    return jnp.concatenate(parts, axis=1)


def restrict(field, tables, weights):
    table_x, table_y = tables
    step = reduce_z(field, weights)
    step = jnp.einsum("caxy,xb->caby", step, table_x, precision=HI)
    return jnp.einsum("caby,yd->cabd", step, table_y, precision=HI)


def invert(diag):
    a, b, c, d, e, f = (diag[0], diag[1], diag[2], diag[3], diag[4], diag[5])
    i00 = b * c - f * f
    i11 = a * c - e * e
    i22 = a * b - d * d
    i01 = e * f - d * c
    i02 = d * f - b * e
    i12 = d * e - a * f
    det = a * i00 + d * i01 + e * i02
    return jnp.stack([i00, i11, i22, i01, i02, i12]) / det


def apply_inverse(inverse, vector):
    out_z = inverse[0] * vector[0] + inverse[3] * vector[1] + inverse[4] * vector[2]
    out_x = inverse[3] * vector[0] + inverse[1] * vector[1] + inverse[5] * vector[2]
    out_y = inverse[4] * vector[0] + inverse[5] * vector[1] + inverse[2] * vector[2]
    return jnp.stack([out_z, out_x, out_y])


def bricks_of(image_slab, deformed_slab):
    both = jnp.concatenate([image_slab, deformed_slab], axis=0)
    n_gx = lax.axis_size("gx")
    fields, nx, ny = both.shape
    bx = nx // n_gx
    blocks = jnp.moveaxis(both.reshape(fields, n_gx, bx, ny), 1, 0)
    brick = lax.all_to_all(blocks, "gx", split_axis=0, concat_axis=0, tiled=True)
    brick = halo(brick, "gy", 3, DMAX)
    brick = halo(brick, "gx", 2, DMAX)
    ny = brick.shape[3]
    image = brick[:, 0]
    deformed = brick[:, 1]
    image_ext = halo(image[:, DMAX - 1 : DMAX + bx + 1, DMAX - 1 : ny - DMAX + 1], "gz", 0, 1)
    deformed_ext = halo(deformed, "gz", 0, DMAX)
    return image_ext, deformed_ext


def shards(image_slab, deformed_slab, shifts):
    image_ext, deformed_ext = bricks_of(image_slab, deformed_slab)
    image = image_ext[1:-1, 1:-1, 1:-1]
    z_count, x_count, y_count = image.shape
    grads = gradients(image_ext)
    tables = (shape_table(x_count), shape_table(y_count))
    tables_sq = (shape_table(x_count, True), shape_table(y_count, True))
    weights = z_weights(False)
    weights_sq = z_weights(True)
    pairs = ((0, 0), (1, 1), (2, 2), (0, 1), (0, 2), (1, 2))

    def residual(moved, warped_now, offset):
        offset_float = offset.astype(jnp.float32)[:, None, None, None]
        return image - warped_now - jnp.sum(grads * (moved - offset_float), axis=0)

    def warp(iteration):
        offset = shifts[iteration, :, 0, 0, 0]
        starts = [DMAX + offset[0], DMAX + offset[1], DMAX + offset[2]]
        return lax.dynamic_slice(deformed_ext, starts, (z_count, x_count, y_count)), offset

    def operator(delta):
        inner = jnp.sum(grads * interpolate(delta, tables, weights), axis=0)
        return share(restrict(grads * inner[None], tables, weights))

    warped, offset = warp(0)
    resid = image - warped + jnp.sum(grads * offset.astype(jnp.float32)[:, None, None, None], axis=0)
    products = jnp.stack([grads[i] * grads[j] for i, j in pairs])
    first = jnp.concatenate(
        [restrict(products, tables_sq, weights_sq), restrict(grads * resid[None], tables, weights)],
        axis=0,
    )
    first = share(first)
    diag = first[:6] + REGULARIZE * jnp.array([1.0, 1.0, 1.0, 0.0, 0.0, 0.0], jnp.float32)[
        :, None, None, None
    ]
    inverse = invert(diag)
    rhs = first[6:]
    nodal = jnp.zeros((3, z_count // ELEMENT + 1, x_count // ELEMENT + 1, y_count // ELEMENT + 1), jnp.float32)
    for iteration in range(ITERS):
        if iteration > 0:
            warped, offset = warp(iteration)
            resid = residual(interpolate(nodal, tables, weights), warped, offset)
            rhs = share(restrict(grads * resid[None], tables, weights))
        delta = DAMPING * apply_inverse(inverse, rhs)
        for sweep in range(SWEEPS - 1):
            applied = operator(delta) + REGULARIZE * delta
            delta = delta + DAMPING * apply_inverse(inverse, rhs - applied)
        nodal = nodal + delta
    final = residual(interpolate(nodal, tables, weights), warped, offset)
    return (nodal, final)


def solution(mesh):
    return jax.shard_map(
        shards,
        mesh=mesh,
        in_specs=(
            P(("gz", "gx"), None, "gy"),
            P(("gz", "gx"), None, "gy"),
            P(None, None, "gz", "gx", "gy"),
        ),
        out_specs=(P(None, "gz", "gx", "gy"), P("gz", "gx", "gy")),
        check_vma=False,
    )
```

```python
import numpy as np

import jax
import jax.numpy as jnp
from jax import lax
from jax.sharding import PartitionSpec as P

ELEMENT = 8
DMAX = 8
ITERS = 2
SWEEPS = 3


DAMPING = 0.7
REGULARIZE = 4.0
HI = lax.Precision.HIGHEST


def shape_table(voxel_count, squared=False):
    voxel = np.arange(voxel_count)
    fraction = ((voxel % ELEMENT).astype(np.float32) + 0.5) / ELEMENT
    owning = voxel // ELEMENT
    nodes = np.arange(voxel_count // ELEMENT + 1)
    lower = (nodes[None, :] == owning[:, None]) * (1.0 - fraction)[:, None]
    upper = (nodes[None, :] == owning[:, None] + 1) * fraction[:, None]
    table = (lower + upper).astype(np.float32)
    if squared:
        table = table * table
    return jnp.asarray(table)


def z_weights(squared=False):
    fraction = (np.arange(ELEMENT, dtype=np.float32) + 0.5) / ELEMENT
    lower = 1.0 - fraction
    if squared:
        return lower * lower, fraction * fraction
    return lower, fraction


def neighbours(axis):
    count = lax.axis_size(axis)
    forward = [(i, i + 1) for i in range(count - 1)]
    backward = [(i + 1, i) for i in range(count - 1)]
    return forward, backward


def halo(block, axis, dim, width):
    forward, backward = neighbours(axis)
    size = block.shape[dim]
    low = lax.ppermute(lax.slice_in_dim(block, size - width, size, axis=dim), axis, forward)
    high = lax.ppermute(lax.slice_in_dim(block, 0, width, axis=dim), axis, backward)
    return jnp.concatenate([low, block, high], axis=dim)


def share(partial_value):
    value = partial_value
    for axis, dim in (("gz", 1), ("gx", 2), ("gy", 3)):
        forward, backward = neighbours(axis)
        size = value.shape[dim]
        first = lax.slice_in_dim(value, 0, 1, axis=dim)
        last = lax.slice_in_dim(value, size - 1, size, axis=dim)
        from_low = lax.ppermute(last, axis, forward)
        from_high = lax.ppermute(first, axis, backward)
        middle = lax.slice_in_dim(value, 1, size - 1, axis=dim)
        value = jnp.concatenate([first + from_low, middle, last + from_high], axis=dim)
    return value


def cut_range(array, axis, start, length):
    return lax.slice_in_dim(array, start, start + length, axis=axis)


def smooth(array, axis):
    length = array.shape[axis] - 2
    return (
        cut_range(array, axis, 0, length)
        + 2.0 * cut_range(array, axis, 1, length)
        + cut_range(array, axis, 2, length)
    ) * 0.25


def differ(array, axis):
    length = array.shape[axis] - 2
    return (cut_range(array, axis, 2, length) - cut_range(array, axis, 0, length)) * 0.5


def gradients(extended):
    along_z = smooth(smooth(differ(extended, 0), 1), 2)
    along_x = smooth(smooth(differ(extended, 1), 0), 2)
    along_y = smooth(smooth(differ(extended, 2), 0), 1)
    return jnp.stack([along_z, along_x, along_y])


def interp_xy(nodal, table_x, table_y):
    step = jnp.einsum("cabd,yd->caby", nodal, table_y, precision=HI)
    return jnp.einsum("caby,xb->caxy", step, table_x, precision=HI)


def expand_z(values, weights):
    lower, upper = weights
    count = values.shape[1] - 1
    low = values[:, :count, None]
    high = values[:, 1:, None]
    shape = (1, 1, ELEMENT, 1, 1)
    joined = low * lower.reshape(shape) + high * upper.reshape(shape)
    return joined.reshape((values.shape[0], count * ELEMENT) + values.shape[2:])


def interpolate(nodal, tables, weights):
    return expand_z(interp_xy(nodal, *tables), weights)


def reduce_z(field, weights):
    lower, upper = weights
    count = field.shape[1] // ELEMENT
    blocks = field.reshape((field.shape[0], count, ELEMENT) + field.shape[2:])
    shape = (1, 1, ELEMENT, 1, 1)
    low = jnp.sum(blocks * lower.reshape(shape), axis=2)
    high = jnp.sum(blocks * upper.reshape(shape), axis=2)
    parts = [low[:, :1]]
    for e in range(1, count):
        parts.append(high[:, e - 1 : e] + low[:, e : e + 1])
    parts.append(high[:, count - 1 :])
    return jnp.concatenate(parts, axis=1)


def restrict(field, tables, weights):
    table_x, table_y = tables
    step = reduce_z(field, weights)
    step = jnp.einsum("caxy,xb->caby", step, table_x, precision=HI)
    return jnp.einsum("caby,yd->cabd", step, table_y, precision=HI)


def invert(diag):
    a, b, c, d, e, f = (diag[0], diag[1], diag[2], diag[3], diag[4], diag[5])
    i00 = b * c - f * f
    i11 = a * c - e * e
    i22 = a * b - d * d
    i01 = e * f - d * c
    i02 = d * f - b * e
    i12 = d * e - a * f
    det = a * i00 + d * i01 + e * i02
    return jnp.stack([i00, i11, i22, i01, i02, i12]) / det


def apply_inverse(inverse, vector):
    out_z = inverse[0] * vector[0] + inverse[3] * vector[1] + inverse[4] * vector[2]
    out_x = inverse[3] * vector[0] + inverse[1] * vector[1] + inverse[5] * vector[2]
    out_y = inverse[4] * vector[0] + inverse[5] * vector[1] + inverse[2] * vector[2]
    return jnp.stack([out_z, out_x, out_y])


def bricks_of(image_slab, deformed_slab):
    both = jnp.concatenate([image_slab, deformed_slab], axis=0)
    n_gx = lax.axis_size("gx")
    fields, nx, ny = both.shape
    bx = nx // n_gx
    main = both.reshape(fields, n_gx, bx, ny)
    zero = jnp.zeros((fields, 1, DMAX, ny), both.dtype)
    low = jnp.concatenate([zero, main[:, :-1, bx - DMAX :]], axis=1)
    high = jnp.concatenate([main[:, 1:, :DMAX], zero], axis=1)
    windows = jnp.concatenate([low, main, high], axis=2)
    windows = jnp.moveaxis(windows, 1, 0)
    brick = lax.all_to_all(windows, "gx", split_axis=0, concat_axis=0, tiled=True)
    brick = halo(brick, "gy", 3, DMAX)
    ny = brick.shape[3]
    forward, backward = neighbours("gz")
    bz = brick.shape[0]
    image = brick[:, 0]
    deformed = brick[:, 1]
    to_high = jnp.concatenate([deformed[bz - DMAX :], image[bz - 1 :]], axis=0)
    to_low = jnp.concatenate([deformed[:DMAX], image[:1]], axis=0)
    from_low = lax.ppermute(to_high, "gz", forward)
    from_high = lax.ppermute(to_low, "gz", backward)
    deformed_ext = jnp.concatenate([from_low[:DMAX], deformed, from_high[:DMAX]], axis=0)
    image_ext = jnp.concatenate([from_low[DMAX:], image, from_high[DMAX:]], axis=0)
    image_ext = image_ext[:, DMAX - 1 : DMAX + bx + 1, DMAX - 1 : ny - DMAX + 1]
    return image_ext, deformed_ext


def shards(image_slab, deformed_slab, shifts):
    image_ext, deformed_ext = bricks_of(image_slab, deformed_slab)
    image = image_ext[1:-1, 1:-1, 1:-1]
    z_count, x_count, y_count = image.shape
    grads = gradients(image_ext)
    tables = (shape_table(x_count), shape_table(y_count))
    tables_sq = (shape_table(x_count, True), shape_table(y_count, True))
    weights = z_weights(False)
    weights_sq = z_weights(True)
    pairs = ((0, 0), (1, 1), (2, 2), (0, 1), (0, 2), (1, 2))

    def residual(moved, warped_now, offset):
        offset_float = offset.astype(jnp.float32)[:, None, None, None]
        return image - warped_now - jnp.sum(grads * (moved - offset_float), axis=0)

    def warp(iteration):
        offset = shifts[iteration, :, 0, 0, 0]
        starts = [DMAX + offset[0], DMAX + offset[1], DMAX + offset[2]]
        return lax.dynamic_slice(deformed_ext, starts, (z_count, x_count, y_count)), offset

    def operator(delta):
        inner = jnp.sum(grads * interpolate(delta, tables, weights), axis=0)
        return share(restrict(grads * inner[None], tables, weights))

    warped, offset = warp(0)
    resid = image - warped + jnp.sum(grads * offset.astype(jnp.float32)[:, None, None, None], axis=0)
    products = jnp.stack([grads[i] * grads[j] for i, j in pairs])
    first = jnp.concatenate(
        [restrict(products, tables_sq, weights_sq), restrict(grads * resid[None], tables, weights)],
        axis=0,
    )
    first = share(first)
    diag = first[:6] + REGULARIZE * jnp.array([1.0, 1.0, 1.0, 0.0, 0.0, 0.0], jnp.float32)[
        :, None, None, None
    ]
    inverse = invert(diag)
    rhs = first[6:]
    nodal = jnp.zeros((3, z_count // ELEMENT + 1, x_count // ELEMENT + 1, y_count // ELEMENT + 1), jnp.float32)
    for iteration in range(ITERS):
        if iteration > 0:
            warped, offset = warp(iteration)
            resid = residual(interpolate(nodal, tables, weights), warped, offset)
            rhs = share(restrict(grads * resid[None], tables, weights))
        delta = DAMPING * apply_inverse(inverse, rhs)
        for sweep in range(SWEEPS - 1):
            applied = operator(delta) + REGULARIZE * delta
            delta = delta + DAMPING * apply_inverse(inverse, rhs - applied)
        nodal = nodal + delta
    final = residual(interpolate(nodal, tables, weights), warped, offset)
    return (nodal, final)


def solution(mesh):
    return jax.shard_map(
        shards,
        mesh=mesh,
        in_specs=(
            P(("gz", "gx"), None, "gy"),
            P(("gz", "gx"), None, "gy"),
            P(None, None, "gz", "gx", "gy"),
        ),
        out_specs=(P(None, "gz", "gx", "gy"), P("gz", "gx", "gy")),
        check_vma=False,
    )
```
